1024 devices in a mesh: gx: 8 (over y, x_lo), gy: 4 (over x_hi, core), gz: 32 (over z).
Axes of the slice: x: 4 (x_hi: 2, x_lo: 2; x = x_hi * 2 + x_lo), y: 4, z: 32, core: 2. Of those that a mesh axis runs over, the one named last changes fastest.
Arguments:
- vorticity: float32 [8, 4, 32, 32768], P('gx', 'gy', 'gz'), may hold values from -6 to 6
- green_spectrum: float32 [64, 4096], replicated, may hold values from 0.05 to 1
- coupling: float32 [2, 2, 2], replicated, may hold values from 0.5 to 1.5
Outputs:
- potential: float32 [8, 4, 32, 32768], P('gx', 'gy', 'gz')
The draws below stay inside these ranges and needn't reach their ends.
All inputs are finite; a program needn't handle non-finite values.
Results may differ from the reference program's by a relative error of at most 0.0015.
Values sent between devices are 32-bit elements; how exact they have to be, the bound alone decides.
No kernel may reach another device: no remote copies, remote signals or barrier semaphores. Data moves between devices by JAX's collectives and lax.ppermute only.
A program may use at most 32 MiB of HBM per device.

```python
import math
import jax
import jax.numpy as jnp
from jax import lax

PX = 32
PY = 32
PZ = 32
BX = 64
BY = 64
BZ = 64
CB = 16
CX = 2
CY = 2
CZ = 2
NX = 256
NY = 128
NZ = 1024
N_GX = 8
N_GY = 4
N_GZ = 32


def block_scale(own_key, extent, pieces, smallest, top_value):
    factor_of, own = 1.0, jax.random.fold_in(own_key, 6)
    for position, blocks in pieces:
        heights = jnp.exp(jax.random.uniform(jax.random.fold_in(own, position), (blocks,), jnp.float32, smallest / len(pieces), top_value / len(pieces)))
        factor_of = factor_of * jnp.repeat(heights, extent[position] // blocks).reshape([-1 if axis == position else 1 for axis in range(len(extent))])
    return factor_of


def noise(stream_key, shape, spread, limit, split=(), dtype=jnp.bfloat16):
    drawn = jax.random.normal(stream_key, shape, jnp.float32) * spread
    if len(split) > 0:
        drawn = block_scale(stream_key, shape, split, -0.22, 0.18) * drawn
    return jnp.clip(drawn, min=-limit, max=limit).astype(dtype)


def setup_inputs(seed: int = 0) -> dict:
    arg_keys = jax.random.split(jax.random.key(seed), 4)
    vorticity = noise(arg_keys[0], (N_GX, N_GY, N_GZ, PX * PY * PZ), 1.0, 6.0, ((0, 8), (1, 4), (2, 32)), jnp.float32)
    green_spectrum = jnp.clip(jnp.exp(jax.random.uniform(arg_keys[1], (BX, BY * BZ), jnp.float32, math.log(0.05), math.log(1.0))), 0.05, 1.0)
    coupling = jnp.clip(jax.random.uniform(arg_keys[2], (CX, CY, CZ), jnp.float32, 0.5, 1.5), 0.5, 1.5)
    return {"vorticity": vorticity, "green_spectrum": green_spectrum, "coupling": coupling}


def angle_tables(count_out, count_in, offset, length, factor):
    rows = lax.iota(jnp.int32, count_out)[:, None]
    cols = lax.iota(jnp.int32, count_in)[None, :]
    phase = (rows * (cols + offset) % length).astype(jnp.float32) * (2.0 * math.pi / length)
    return ((jnp.cos(phase) * factor).astype(jnp.bfloat16), (jnp.sin(phase) * factor).astype(jnp.bfloat16))

def mixed(form, table, data):
    return jnp.einsum(form, table.astype(jnp.float32), data.astype(jnp.float32), precision=lax.Precision.HIGHEST)

def local_box(patch, green_spectrum):
    bf = jnp.bfloat16
    px, py, pz = patch.shape
    bx, by, bz = green_spectrum.shape
    wb = patch.astype(bf)
    cosx, sinx = angle_tables(bx, px, px // 2, bx, 1.0)
    cosy, siny = angle_tables(by, py, py // 2, by, 1.0)
    cosz, sinz = angle_tables(bz, pz, pz // 2, bz, 1.0)
    real = mixed('kn,nyz->kyz', cosx, wb).astype(bf)
    imag = (-mixed('kn,nyz->kyz', sinx, wb)).astype(bf)
    for form, cosv, sinv in (('ky,xyz->xkz', cosy, siny), ('kz,xyz->xyk', cosz, sinz)):
        new_real = (mixed(form, cosv, real) + mixed(form, sinv, imag)).astype(bf)
        imag = (mixed(form, cosv, imag) - mixed(form, sinv, real)).astype(bf)
        real = new_real
    real = (real.astype(jnp.float32) * green_spectrum).astype(bf)
    imag = (imag.astype(jnp.float32) * green_spectrum).astype(bf)
    icosz, isinz = angle_tables(bz, bz, 0, bz, 1.0 / bz)
    icosy, isiny = angle_tables(by, by, 0, by, 1.0 / by)
    icosx, isinx = angle_tables(bx, bx, 0, bx, 1.0 / bx)
    for form, cosv, sinv in (('nk,xyk->xyn', icosz, isinz), ('nk,xkz->xnz', icosy, isiny)):
        new_real = (mixed(form, cosv, real) - mixed(form, sinv, imag)).astype(bf)
        imag = (mixed(form, cosv, imag) + mixed(form, sinv, real)).astype(bf)
        real = new_real
    return mixed('nk,kyz->nyz', icosx, real) - mixed('nk,kyz->nyz', isinx, imag)

def reference(vorticity, green_spectrum, coupling):
    count = N_GX * N_GY * N_GZ
    spectrum = green_spectrum.reshape(BX, BY, BZ)
    patches = vorticity.reshape(count, PX, PY, PZ)
    grid = jnp.zeros((NX + PX, NY + PY, NZ + PZ), jnp.float32)

    def add_patch(index, grid):
        box = local_box(patches[index], spectrum)
        ix = (index // (N_GY * N_GZ)).astype(jnp.int32)
        iy = (index // N_GZ % N_GY).astype(jnp.int32)
        iz = (index % N_GZ).astype(jnp.int32)
        starts = (ix * PX, iy * PY, iz * PZ)
        current = lax.dynamic_slice(grid, starts, (BX, BY, BZ))
        return lax.dynamic_update_slice(grid, current + box, starts)
    grid = lax.fori_loop(0, count, add_patch, grid)
    near = grid[PX // 2:PX // 2 + NX, PY // 2:PY // 2 + NY, PZ // 2:PZ // 2 + NZ]
    near = near.reshape(N_GX, PX, N_GY, PY, N_GZ, PZ).transpose(0, 2, 4, 1, 3, 5).reshape(count, PX, PY, PZ)
    scale = 1.0 / math.sqrt(CB ** 3)
    coarse = patches.reshape(count, CX, CB, CY, CB, CZ, CB).sum(axis=(2, 4, 6)) * scale
    coarse = coarse.reshape(count, CX * CY * CZ)
    levels = count.bit_length() - 1
    total = jnp.zeros_like(coarse)
    for level in range(1, levels + 1):
        group = 2 ** level
        sums = coarse.reshape(count // group, group, -1).sum(axis=1) / math.sqrt(group)
        total = total + jnp.repeat(sums, group, axis=0)
    far = total.reshape(count, CX, CY, CZ) * coupling
    far = jnp.repeat(jnp.repeat(jnp.repeat(far, CB, axis=1), CB, axis=2), CB, axis=3)
    return (near + far).reshape(N_GX, N_GY, N_GZ, PX * PY * PZ)
```

```python
import math

import jax
import jax.numpy as jnp
from jax import lax
from jax.sharding import PartitionSpec as P

PX = 32
PY = 32
PZ = 32
CB = 16


def from_behind(block, axis, distance):
    devices = range(lax.axis_size(axis))
    route = [(i - distance, i) for i in devices if i - distance in devices]
    return lax.ppermute(block, axis, route)


def from_partner(value, axis, apart):
    mask = 2**apart
    pairs = [(source, source ^ mask) for source in range(lax.axis_size(axis))]
    return lax.ppermute(value, axis, pairs)


def angle_tables(count_out, count_in, offset, length, factor):
    rows = lax.iota(jnp.int32, count_out)[:, None]
    cols = lax.iota(jnp.int32, count_in)[None, :]
    phase = (rows * (cols + offset) % length).astype(jnp.float32) * (2.0 * math.pi / length)
    return (
        (jnp.cos(phase) * factor).astype(jnp.bfloat16),
        (jnp.sin(phase) * factor).astype(jnp.bfloat16),
    )


def mixed(form, table, data):
    return jnp.einsum(form, table, data, preferred_element_type=jnp.float32)


def local_box(patch, green_spectrum):
    bf = jnp.bfloat16
    px, py, pz = patch.shape
    bx, by, bz = green_spectrum.shape
    wb = patch.astype(bf)
    cosx, sinx = angle_tables(bx, px, px // 2, bx, 1.0)
    cosy, siny = angle_tables(by, py, py // 2, by, 1.0)
    cosz, sinz = angle_tables(bz, pz, pz // 2, bz, 1.0)
    real = mixed("kn,nyz->kyz", cosx, wb).astype(bf)
    imag = (-mixed("kn,nyz->kyz", sinx, wb)).astype(bf)
    for form, cosv, sinv in (("ky,xyz->xkz", cosy, siny), ("kz,xyz->xyk", cosz, sinz)):
        new_real = (mixed(form, cosv, real) + mixed(form, sinv, imag)).astype(bf)
        imag = (mixed(form, cosv, imag) - mixed(form, sinv, real)).astype(bf)
        real = new_real
    real = (real.astype(jnp.float32) * green_spectrum).astype(bf)
    imag = (imag.astype(jnp.float32) * green_spectrum).astype(bf)
    icosz, isinz = angle_tables(bz, bz, 0, bz, 1.0 / bz)
    icosy, isiny = angle_tables(by, by, 0, by, 1.0 / by)
    icosx, isinx = angle_tables(bx, bx, 0, bx, 1.0 / bx)
    for form, cosv, sinv in (("nk,xyk->xyn", icosz, isinz), ("nk,xkz->xnz", icosy, isiny)):
        new_real = (mixed(form, cosv, real) - mixed(form, sinv, imag)).astype(bf)
        imag = (mixed(form, cosv, imag) + mixed(form, sinv, real)).astype(bf)
        real = new_real
    return mixed("nk,kyz->nyz", icosx, real) - mixed("nk,kyz->nyz", isinx, imag)


def move_x(part, step):
    return from_behind(part, "gx", step)


def move_y(part, step):
    return from_behind(part, "gy", step)


def move_z(part, step):
    return from_behind(part, "gz", step)


def fold_margin(field, dim, mover):
    quarter = field.shape[dim] // 4
    low_rim = lax.slice_in_dim(field, 0, quarter, axis=dim)
    first = lax.slice_in_dim(field, quarter, 2 * quarter, axis=dim)
    second = lax.slice_in_dim(field, 2 * quarter, 3 * quarter, axis=dim)
    high_rim = lax.slice_in_dim(field, 3 * quarter, 4 * quarter, axis=dim)
    low_rim, high_rim = lax.optimization_barrier((low_rim, high_rim))
    from_left = mover(high_rim, 1)
    from_right = mover(low_rim, -1)
    return jnp.concatenate([first + from_left, second + from_right], axis=dim)


def far_sum(flat):
    nz, ny, nx = (lax.axis_size("gz"), lax.axis_size("gy"), lax.axis_size("gx"))
    c, b, a = (lax.axis_index("gz"), lax.axis_index("gy"), lax.axis_index("gx"))
    zslots = lax.iota(jnp.int32, nz)
    line = lax.psum(jnp.where((zslots == c)[:, None], flat[None, :], 0.0), "gz")
    ab = a * ny + b
    abslots = lax.iota(jnp.int32, nx * ny)
    plane = lax.psum(jnp.where((abslots == ab)[:, None], flat[None, :], 0.0), ("gx", "gy", "gz"))
    total = jnp.zeros_like(flat)
    zlevels = nz.bit_length() - 1
    for level in range(1, zlevels + 1):
        mask = (zslots >> level) == (c >> level)
        total = total + jnp.sum(jnp.where(mask[:, None], line, 0.0), axis=0) / math.sqrt(2**level)
    for level in range(1, (nx * ny).bit_length()):
        mask = (abslots >> level) == (ab >> level)
        group = 2 ** (level + zlevels)
        total = total + jnp.sum(jnp.where(mask[:, None], plane, 0.0), axis=0) / math.sqrt(group)
    return total


def local(vorticity, green_spectrum, coupling):
    px, py, pz = (PX, PY, PZ)
    patch = vorticity.reshape(px, py, pz)
    spectrum = green_spectrum.reshape(2 * px, 2 * py, 2 * pz)
    box = local_box(patch, spectrum)
    order = ((2, move_z), (1, move_y), (0, move_x))
    near = box
    for dim, mover in order:
        near = fold_margin(near, dim, mover)
    cx, cy, cz = (px // CB, py // CB, pz // CB)
    scale = 1.0 / math.sqrt(CB**3)
    coarse = patch.reshape(cx, CB, cy, CB, cz, CB).sum(axis=(1, 3, 5)) * scale
    flat = coarse.reshape(-1)
    total = far_sum(flat)
    far = total.reshape(cx, cy, cz) * coupling
    far_cells = jnp.broadcast_to(far[:, None, :, None, :, None], (cx, CB, cy, CB, cz, CB)).reshape(
        px, py, pz
    )
    return (near + far_cells).reshape(1, 1, 1, px * py * pz)


def solution(mesh):
    return jax.shard_map(
        local,
        mesh=mesh,
        in_specs=(P("gx", "gy", "gz", None), P(), P()),
        out_specs=P("gx", "gy", "gz", None),
        check_vma=False,
    )
```

```python
import math

import jax
import jax.numpy as jnp
from jax import lax
from jax.sharding import PartitionSpec as P

PX = 32
PY = 32
PZ = 32
CB = 16


def from_behind(block, axis, distance):
    devices = range(lax.axis_size(axis))
    route = [(i - distance, i) for i in devices if i - distance in devices]
    return lax.ppermute(block, axis, route)


def from_partner(value, axis, apart):
    mask = 2**apart
    pairs = [(source, source ^ mask) for source in range(lax.axis_size(axis))]
    return lax.ppermute(value, axis, pairs)


def angle_tables(count_out, count_in, offset, length, factor):
    rows = lax.iota(jnp.int32, count_out)[:, None]
    cols = lax.iota(jnp.int32, count_in)[None, :]
    phase = (rows * (cols + offset) % length).astype(jnp.float32) * (2.0 * math.pi / length)
    return (
        (jnp.cos(phase) * factor).astype(jnp.bfloat16),
        (jnp.sin(phase) * factor).astype(jnp.bfloat16),
    )


def mixed(form, table, data):
    return jnp.einsum(form, table, data, preferred_element_type=jnp.float32)


def local_box(patch, green_spectrum):
    bf = jnp.bfloat16
    px, py, pz = patch.shape
    bx, by, bz = green_spectrum.shape
    wb = patch.astype(bf)
    cosx, sinx = angle_tables(bx, px, px // 2, bx, 1.0)
    cosy, siny = angle_tables(by, py, py // 2, by, 1.0)
    cosz, sinz = angle_tables(bz, pz, pz // 2, bz, 1.0)
    real = mixed("kn,nyz->kyz", cosx, wb).astype(bf)
    imag = (-mixed("kn,nyz->kyz", sinx, wb)).astype(bf)
    for form, cosv, sinv in (("ky,xyz->xkz", cosy, siny), ("kz,xyz->xyk", cosz, sinz)):
        new_real = (mixed(form, cosv, real) + mixed(form, sinv, imag)).astype(bf)
        imag = (mixed(form, cosv, imag) - mixed(form, sinv, real)).astype(bf)
        real = new_real
    real = (real.astype(jnp.float32) * green_spectrum).astype(bf)
    imag = (imag.astype(jnp.float32) * green_spectrum).astype(bf)
    icosz, isinz = angle_tables(bz, bz, 0, bz, 1.0 / bz)
    icosy, isiny = angle_tables(by, by, 0, by, 1.0 / by)
    icosx, isinx = angle_tables(bx, bx, 0, bx, 1.0 / bx)
    for form, cosv, sinv in (("nk,xyk->xyn", icosz, isinz), ("nk,xkz->xnz", icosy, isiny)):
        new_real = (mixed(form, cosv, real) - mixed(form, sinv, imag)).astype(bf)
        imag = (mixed(form, cosv, imag) + mixed(form, sinv, real)).astype(bf)
        real = new_real
    return mixed("nk,kyz->nyz", icosx, real) - mixed("nk,kyz->nyz", isinx, imag)


def move_x(part, step):
    return from_behind(part, "gx", step)


def move_y(part, step):
    return from_behind(part, "gy", step)


def move_z(part, step):
    return from_behind(part, "gz", step)


def fold_margin(field, dim, mover):
    quarter = field.shape[dim] // 4
    low_rim = lax.slice_in_dim(field, 0, quarter, axis=dim)
    first = lax.slice_in_dim(field, quarter, 2 * quarter, axis=dim)
    second = lax.slice_in_dim(field, 2 * quarter, 3 * quarter, axis=dim)
    high_rim = lax.slice_in_dim(field, 3 * quarter, 4 * quarter, axis=dim)
    low_rim, high_rim = lax.optimization_barrier((low_rim, high_rim))
    from_left = mover(high_rim, 1)
    from_right = mover(low_rim, -1)
    return jnp.concatenate([first + from_left, second + from_right], axis=dim)


def far_sum(flat):
    axes = ("gx", "gy", "gz")
    count = lax.axis_size(axes)
    me = lax.axis_index(axes)
    slots = lax.iota(jnp.int32, count)
    table = jnp.where((slots == me)[:, None], flat[None, :], 0.0)
    table = jnp.concatenate([table, jnp.zeros_like(table)], axis=0)
    table = lax.psum(table, axes)[:count]
    total = jnp.zeros_like(flat)
    for level in range(1, count.bit_length()):
        mask = (slots >> level) == (me >> level)
        total = total + jnp.sum(jnp.where(mask[:, None], table, 0.0), axis=0) / math.sqrt(2**level)
    return total


def local(vorticity, green_spectrum, coupling):
    px, py, pz = (PX, PY, PZ)
    patch = vorticity.reshape(px, py, pz)
    spectrum = green_spectrum.reshape(2 * px, 2 * py, 2 * pz)
    box = local_box(patch, spectrum)
    order = ((2, move_z), (1, move_y), (0, move_x))
    near = box
    for dim, mover in order:
        near = fold_margin(near, dim, mover)
    cx, cy, cz = (px // CB, py // CB, pz // CB)
    scale = 1.0 / math.sqrt(CB**3)
    coarse = patch.reshape(cx, CB, cy, CB, cz, CB).sum(axis=(1, 3, 5)) * scale
    flat = coarse.reshape(-1)
    total = far_sum(flat)
    far = total.reshape(cx, cy, cz) * coupling
    far_cells = jnp.broadcast_to(far[:, None, :, None, :, None], (cx, CB, cy, CB, cz, CB)).reshape(
        px, py, pz
    )
    return (near + far_cells).reshape(1, 1, 1, px * py * pz)


def solution(mesh):
    return jax.shard_map(
        local,
        mesh=mesh,
        in_specs=(P("gx", "gy", "gz", None), P(), P()),
        out_specs=P("gx", "gy", "gz", None),
        check_vma=False,
    )
```

```python
import math

import jax
import jax.numpy as jnp
from jax import lax
from jax.sharding import PartitionSpec as P

PX = 32
PY = 32
PZ = 32
CB = 16


def from_behind(block, axis, distance):
    devices = range(lax.axis_size(axis))
    route = [(i - distance, i) for i in devices if i - distance in devices]
    return lax.ppermute(block, axis, route)


def from_partner(value, axis, apart):
    mask = 2**apart
    pairs = [(source, source ^ mask) for source in range(lax.axis_size(axis))]
    return lax.ppermute(value, axis, pairs)


def angle_tables(count_out, count_in, offset, length, factor):
    rows = lax.iota(jnp.int32, count_out)[:, None]
    cols = lax.iota(jnp.int32, count_in)[None, :]
    phase = (rows * (cols + offset) % length).astype(jnp.float32) * (2.0 * math.pi / length)
    return (
        (jnp.cos(phase) * factor).astype(jnp.bfloat16),
        (jnp.sin(phase) * factor).astype(jnp.bfloat16),
    )


def mixed(form, table, data):
    return jnp.einsum(form, table, data, preferred_element_type=jnp.float32)


def local_box(patch, green_spectrum):
    bf = jnp.bfloat16
    px, py, pz = patch.shape
    bx, by, bz = green_spectrum.shape
    wb = patch.astype(bf)
    cosx, sinx = angle_tables(bx, px, px // 2, bx, 1.0)
    cosy, siny = angle_tables(by, py, py // 2, by, 1.0)
    cosz, sinz = angle_tables(bz, pz, pz // 2, bz, 1.0)
    real = mixed("kn,nyz->kyz", cosx, wb).astype(bf)
    imag = (-mixed("kn,nyz->kyz", sinx, wb)).astype(bf)
    for form, cosv, sinv in (("ky,xyz->xkz", cosy, siny), ("kz,xyz->xyk", cosz, sinz)):
        new_real = (mixed(form, cosv, real) + mixed(form, sinv, imag)).astype(bf)
        imag = (mixed(form, cosv, imag) - mixed(form, sinv, real)).astype(bf)
        real = new_real
    real = (real.astype(jnp.float32) * green_spectrum).astype(bf)
    imag = (imag.astype(jnp.float32) * green_spectrum).astype(bf)
    icosz, isinz = angle_tables(bz, bz, 0, bz, 1.0 / bz)
    icosy, isiny = angle_tables(by, by, 0, by, 1.0 / by)
    icosx, isinx = angle_tables(bx, bx, 0, bx, 1.0 / bx)
    for form, cosv, sinv in (("nk,xyk->xyn", icosz, isinz), ("nk,xkz->xnz", icosy, isiny)):
        new_real = (mixed(form, cosv, real) - mixed(form, sinv, imag)).astype(bf)
        imag = (mixed(form, cosv, imag) + mixed(form, sinv, real)).astype(bf)
        real = new_real
    return mixed("nk,kyz->nyz", icosx, real) - mixed("nk,kyz->nyz", isinx, imag)


def move_x(part, step):
    return from_behind(part, "gx", step)


def move_y(part, step):
    return from_behind(part, "gy", step)


def move_z(part, step):
    return from_behind(part, "gz", step)


def fold_margin(field, dim, mover):
    quarter = field.shape[dim] // 4
    low_rim = lax.slice_in_dim(field, 0, quarter, axis=dim)
    first = lax.slice_in_dim(field, quarter, 2 * quarter, axis=dim)
    second = lax.slice_in_dim(field, 2 * quarter, 3 * quarter, axis=dim)
    high_rim = lax.slice_in_dim(field, 3 * quarter, 4 * quarter, axis=dim)
    low_rim, high_rim = lax.optimization_barrier((low_rim, high_rim))
    from_left = mover(high_rim, 1)
    from_right = mover(low_rim, -1)
    return jnp.concatenate([first + from_left, second + from_right], axis=dim)


def gather_rows(value, axes):
    count = lax.axis_size(axes)
    rows = jnp.broadcast_to(value[None, :], (count, value.shape[0]))
    return lax.all_to_all(rows, axes, 0, 0, tiled=True)


def level_sums(rows, me, first_level, group_of):
    slots = lax.iota(jnp.int32, rows.shape[0])
    total = jnp.zeros(rows.shape[1:], rows.dtype)
    for level in range(1, rows.shape[0].bit_length()):
        mask = (slots >> level) == (me >> level)
        total = total + jnp.sum(jnp.where(mask[:, None], rows, 0.0), axis=0) / math.sqrt(group_of(level))
    return total


def far_sum(flat):
    nz = lax.axis_size("gz")
    zlevels = nz.bit_length() - 1
    line = gather_rows(flat, "gz")
    total = level_sums(line, lax.axis_index("gz"), 1, lambda level: 2**level)
    line_sum = jnp.sum(line, axis=0)
    plane = gather_rows(line_sum, ("gx", "gy"))
    ab = lax.axis_index(("gx", "gy"))
    return total + level_sums(plane, ab, 1, lambda level: 2 ** (level + zlevels))


def local(vorticity, green_spectrum, coupling):
    px, py, pz = (PX, PY, PZ)
    patch = vorticity.reshape(px, py, pz)
    spectrum = green_spectrum.reshape(2 * px, 2 * py, 2 * pz)
    box = local_box(patch, spectrum)
    order = ((2, move_z), (1, move_y), (0, move_x))
    near = box
    for dim, mover in order:
        near = fold_margin(near, dim, mover)
    cx, cy, cz = (px // CB, py // CB, pz // CB)
    scale = 1.0 / math.sqrt(CB**3)
    coarse = patch.reshape(cx, CB, cy, CB, cz, CB).sum(axis=(1, 3, 5)) * scale
    flat = coarse.reshape(-1)
    total = far_sum(flat)
    far = total.reshape(cx, cy, cz) * coupling
    far_cells = jnp.broadcast_to(far[:, None, :, None, :, None], (cx, CB, cy, CB, cz, CB)).reshape(
        px, py, pz
    )
    return (near + far_cells).reshape(1, 1, 1, px * py * pz)


def solution(mesh):
    return jax.shard_map(
        local,
        mesh=mesh,
        in_specs=(P("gx", "gy", "gz", None), P(), P()),
        out_specs=P("gx", "gy", "gz", None),
        check_vma=False,
    )
```

```python
import math

import jax
import jax.numpy as jnp
from jax import lax
from jax.sharding import PartitionSpec as P


PX = 32
PY = 32
PZ = 32
CB = 16


def from_behind(block, axis, distance):
    devices = range(lax.axis_size(axis))
    route = [(i - distance, i) for i in devices if i - distance in devices]
    return lax.ppermute(block, axis, route)


def angle_tables(count_out, count_in, offset, length, factor):
    rows = lax.iota(jnp.int32, count_out)[:, None]
    cols = lax.iota(jnp.int32, count_in)[None, :]
    phase = (rows * (cols + offset) % length).astype(jnp.float32) * (2.0 * math.pi / length)
    return (
        (jnp.cos(phase) * factor).astype(jnp.bfloat16),
        (jnp.sin(phase) * factor).astype(jnp.bfloat16),
    )


def mixed(form, table, data):
    return jnp.einsum(form, table, data, preferred_element_type=jnp.float32)


def local_box(patch, green_spectrum):
    bf = jnp.bfloat16
    px, py, pz = patch.shape
    bx, by, bz = green_spectrum.shape
    wb = patch.astype(bf)
    cosx, sinx = angle_tables(bx, px, px // 2, bx, 1.0)
    cosy, siny = angle_tables(by, py, py // 2, by, 1.0)
    cosz, sinz = angle_tables(bz, pz, pz // 2, bz, 1.0)
    real = mixed("kn,nyz->kyz", cosx, wb).astype(bf)
    imag = (-mixed("kn,nyz->kyz", sinx, wb)).astype(bf)
    for form, cosv, sinv in (("ky,xyz->xkz", cosy, siny), ("kz,xyz->xyk", cosz, sinz)):
        new_real = (mixed(form, cosv, real) + mixed(form, sinv, imag)).astype(bf)
        imag = (mixed(form, cosv, imag) - mixed(form, sinv, real)).astype(bf)
        real = new_real
    real = (real.astype(jnp.float32) * green_spectrum).astype(bf)
    imag = (imag.astype(jnp.float32) * green_spectrum).astype(bf)
    icosz, isinz = angle_tables(bz, bz, 0, bz, 1.0 / bz)
    icosy, isiny = angle_tables(by, by, 0, by, 1.0 / by)
    icosx, isinx = angle_tables(bx, bx, 0, bx, 1.0 / bx)
    for form, cosv, sinv in (("nk,xyk->xyn", icosz, isinz), ("nk,xkz->xnz", icosy, isiny)):
        new_real = (mixed(form, cosv, real) - mixed(form, sinv, imag)).astype(bf)
        imag = (mixed(form, cosv, imag) + mixed(form, sinv, real)).astype(bf)
        real = new_real
    return mixed("nk,kyz->nyz", icosx, real) - mixed("nk,kyz->nyz", isinx, imag)


def move_x(part, step):
    return from_behind(part, "gx", step)


def move_y(part, step):
    return from_behind(part, "gy", step)


def move_z(part, step):
    return from_behind(part, "gz", step)


def fold_margin(field, dim, mover):
    quarter = field.shape[dim] // 4
    low_rim = lax.slice_in_dim(field, 0, quarter, axis=dim)
    first = lax.slice_in_dim(field, quarter, 2 * quarter, axis=dim)
    second = lax.slice_in_dim(field, 2 * quarter, 3 * quarter, axis=dim)
    high_rim = lax.slice_in_dim(field, 3 * quarter, 4 * quarter, axis=dim)
    low_rim, high_rim = lax.optimization_barrier((low_rim, high_rim))
    from_left = mover(high_rim, 1)
    from_right = mover(low_rim, -1)
    return jnp.concatenate([first + from_left, second + from_right], axis=dim)


def gather_rows(value, axes):
    count = lax.axis_size(axes)
    rows = jnp.broadcast_to(value[None, :], (count, value.shape[0]))
    return lax.all_to_all(rows, axes, 0, 0, tiled=True)


def level_sums(rows, me, group_of):
    slots = lax.iota(jnp.int32, rows.shape[0])
    total = jnp.zeros(rows.shape[1:], rows.dtype)
    for level in range(1, rows.shape[0].bit_length()):
        mask = (slots >> level) == (me >> level)
        total = total + jnp.sum(jnp.where(mask[:, None], rows, 0.0), axis=0) / math.sqrt(group_of(level))
    return total


def far_sum(flat):
    nz = lax.axis_size("gz")
    zlevels = nz.bit_length() - 1
    line = gather_rows(flat, "gz")
    total = level_sums(line, lax.axis_index("gz"), lambda level: 2**level)
    line_sum = jnp.sum(line, axis=0)
    plane = gather_rows(line_sum, ("gx", "gy"))
    ab = lax.axis_index(("gx", "gy"))
    return total + level_sums(plane, ab, lambda level: 2 ** (level + zlevels))


def local(vorticity, green_spectrum, coupling):
    px, py, pz = (PX, PY, PZ)
    patch = vorticity.reshape(px, py, pz)
    spectrum = green_spectrum.reshape(2 * px, 2 * py, 2 * pz)
    box = local_box(patch, spectrum)
    order = ((2, move_z), (1, move_y), (0, move_x))
    near = box
    for dim, mover in order:
        near = fold_margin(near, dim, mover)
    cx, cy, cz = (px // CB, py // CB, pz // CB)
    scale = 1.0 / math.sqrt(CB**3)
    coarse = patch.reshape(cx, CB, cy, CB, cz, CB).sum(axis=(1, 3, 5)) * scale
    flat = coarse.reshape(-1)
    total = far_sum(flat)
    far = total.reshape(cx, cy, cz) * coupling
    far_cells = jnp.broadcast_to(far[:, None, :, None, :, None], (cx, CB, cy, CB, cz, CB)).reshape(
        px, py, pz
    )
    return (near + far_cells).reshape(1, 1, 1, px * py * pz)


def solution(mesh):
    return jax.shard_map(
        local,
        mesh=mesh,
        in_specs=(P("gx", "gy", "gz", None), P(), P()),
        out_specs=P("gx", "gy", "gz", None),
        check_vma=False,
    )
```

```python
import math

import jax
import jax.numpy as jnp
from jax import lax
from jax.sharding import PartitionSpec as P

PX = 32
PY = 32
PZ = 32
CB = 16


def from_behind(block, axis, distance):
    devices = range(lax.axis_size(axis))
    route = [(i - distance, i) for i in devices if i - distance in devices]
    return lax.ppermute(block, axis, route)


def from_partner(value, axis, apart):
    mask = 2**apart
    pairs = [(source, source ^ mask) for source in range(lax.axis_size(axis))]
    return lax.ppermute(value, axis, pairs)


def angle_tables(count_out, count_in, offset, length, factor):
    rows = lax.iota(jnp.int32, count_out)[:, None]
    cols = lax.iota(jnp.int32, count_in)[None, :]
    phase = (rows * (cols + offset) % length).astype(jnp.float32) * (2.0 * math.pi / length)
    return (
        (jnp.cos(phase) * factor).astype(jnp.bfloat16),
        (jnp.sin(phase) * factor).astype(jnp.bfloat16),
    )


def mixed(form, table, data):
    return jnp.einsum(form, table, data, preferred_element_type=jnp.float32)


def forward_stage(form, table_cos, table_sin, parts):
    table = jnp.concatenate([table_cos.T, table_sin.T], axis=1)
    half = table_cos.shape[0]
    prods = [jnp.einsum(form, part, table, preferred_element_type=jnp.float32) for part in parts]
    return [(prod[..., :half], prod[..., half:]) for prod in prods]


def inverse_stage(form, table_cos, table_sin, parts):
    table = jnp.concatenate([table_cos, table_sin], axis=0)
    half = table_cos.shape[0]
    prods = [jnp.einsum(form, table, part, preferred_element_type=jnp.float32) for part in parts]
    return [(prod[:half], prod[half:]) for prod in prods]


def local_box(patch, green_spectrum):
    bf = jnp.bfloat16
    px, py, pz = patch.shape
    bx, by, bz = green_spectrum.shape
    wb = patch.astype(bf)
    cosx, sinx = angle_tables(bx, px, px // 2, bx, 1.0)
    cosy, siny = angle_tables(by, py, py // 2, by, 1.0)
    cosz, sinz = angle_tables(bz, pz, pz // 2, bz, 1.0)
    ((rc, rs),) = forward_stage("xyz,xm->yzm", cosx, -sinx, (wb,))
    real, imag = rc.astype(bf), rs.astype(bf)
    for form, cosv, sinv in (("yzk,ym->zkm", cosy, siny), ("zab,zm->abm", cosz, sinz)):
        (rc, rs), (ic, is_) = forward_stage(form, cosv, sinv, (real, imag))
        real, imag = (rc + is_).astype(bf), (ic - rs).astype(bf)
    real = (real.astype(jnp.float32) * green_spectrum).astype(bf)
    imag = (imag.astype(jnp.float32) * green_spectrum).astype(bf)
    icosz, isinz = angle_tables(bz, bz, 0, bz, 1.0 / bz)
    icosy, isiny = angle_tables(by, by, 0, by, 1.0 / by)
    icosx, isinx = angle_tables(bx, bx, 0, bx, 1.0 / bx)
    for cosv, sinv in ((icosz, isinz), (icosy, isiny)):
        (rc, rs), (ic, is_) = inverse_stage("mk,abk->mab", cosv, sinv, (real, imag))
        real, imag = (rc - is_).astype(bf), (ic + rs).astype(bf)
    (rc, rs), (ic, is_) = inverse_stage("mk,abk->mab", icosx, isinx, (real, imag))
    return rc - is_


def move_x(part, step):
    return from_behind(part, "gx", step)


def move_y(part, step):
    return from_behind(part, "gy", step)


def move_z(part, step):
    return from_behind(part, "gz", step)


def fold_margin(field, dim, mover):
    quarter = field.shape[dim] // 4
    low_rim = lax.slice_in_dim(field, 0, quarter, axis=dim)
    first = lax.slice_in_dim(field, quarter, 2 * quarter, axis=dim)
    second = lax.slice_in_dim(field, 2 * quarter, 3 * quarter, axis=dim)
    high_rim = lax.slice_in_dim(field, 3 * quarter, 4 * quarter, axis=dim)
    low_rim, high_rim = lax.optimization_barrier((low_rim, high_rim))
    from_left = mover(high_rim, 1)
    from_right = mover(low_rim, -1)
    return jnp.concatenate([first + from_left, second + from_right], axis=dim)


def gather_rows(value, axes):
    count = lax.axis_size(axes)
    rows = jnp.broadcast_to(value[None, :], (count, value.shape[0]))
    return lax.all_to_all(rows, axes, 0, 0, tiled=True)


def level_sums(rows, me, first_level, group_of):
    slots = lax.iota(jnp.int32, rows.shape[0])
    total = jnp.zeros(rows.shape[1:], rows.dtype)
    for level in range(1, rows.shape[0].bit_length()):
        mask = (slots >> level) == (me >> level)
        total = total + jnp.sum(jnp.where(mask[:, None], rows, 0.0), axis=0) / math.sqrt(group_of(level))
    return total


def far_sum(flat):
    nz = lax.axis_size("gz")
    zlevels = nz.bit_length() - 1
    line = gather_rows(flat, "gz")
    total = level_sums(line, lax.axis_index("gz"), 1, lambda level: 2**level)
    line_sum = jnp.sum(line, axis=0)
    plane = gather_rows(line_sum, ("gx", "gy"))
    ab = lax.axis_index(("gx", "gy"))
    return total + level_sums(plane, ab, 1, lambda level: 2 ** (level + zlevels))


def local(vorticity, green_spectrum, coupling):
    px, py, pz = (PX, PY, PZ)
    patch = vorticity.reshape(px, py, pz)
    spectrum = green_spectrum.reshape(2 * px, 2 * py, 2 * pz)
    box = local_box(patch, spectrum)
    order = ((2, move_z), (1, move_y), (0, move_x))
    near = box
    for dim, mover in order:
        near = fold_margin(near, dim, mover)
    cx, cy, cz = (px // CB, py // CB, pz // CB)
    scale = 1.0 / math.sqrt(CB**3)
    coarse = patch.reshape(cx, CB, cy, CB, cz, CB).sum(axis=(1, 3, 5)) * scale
    flat = coarse.reshape(-1)
    total = far_sum(flat)
    far = total.reshape(cx, cy, cz) * coupling
    far_cells = jnp.broadcast_to(far[:, None, :, None, :, None], (cx, CB, cy, CB, cz, CB)).reshape(
        px, py, pz
    )
    return (near + far_cells).reshape(1, 1, 1, px * py * pz)


def solution(mesh):
    return jax.shard_map(
        local,
        mesh=mesh,
        in_specs=(P("gx", "gy", "gz", None), P(), P()),
        out_specs=P("gx", "gy", "gz", None),
        check_vma=False,
    )
```

```python
import math

import jax
import jax.numpy as jnp
from jax import lax
from jax.sharding import PartitionSpec as P

PX = 32
PY = 32
PZ = 32
CB = 16


def from_behind(block, axis, distance):
    devices = range(lax.axis_size(axis))
    route = [(i - distance, i) for i in devices if i - distance in devices]
    return lax.ppermute(block, axis, route)


def from_partner(value, axis, apart):
    mask = 2**apart
    pairs = [(source, source ^ mask) for source in range(lax.axis_size(axis))]
    return lax.ppermute(value, axis, pairs)


def angle_tables(count_out, count_in, offset, length, factor):
    rows = lax.iota(jnp.int32, count_out)[:, None]
    cols = lax.iota(jnp.int32, count_in)[None, :]
    phase = (rows * (cols + offset) % length).astype(jnp.float32) * (2.0 * math.pi / length)
    return (
        (jnp.cos(phase) * factor).astype(jnp.bfloat16),
        (jnp.sin(phase) * factor).astype(jnp.bfloat16),
    )


def mixed(form, table, data):
    return jnp.einsum(form, table, data, preferred_element_type=jnp.float32)


def local_box(patch, green_spectrum):
    bf = jnp.bfloat16
    px, py, pz = patch.shape
    bx, by, bz = green_spectrum.shape
    wb = patch.astype(bf)
    cosx, sinx = angle_tables(bx, px, px // 2, bx, 1.0)
    cosy, siny = angle_tables(by, py, py // 2, by, 1.0)
    cosz, sinz = angle_tables(bz, pz, pz // 2, bz, 1.0)
    real = mixed("kn,nyz->kyz", cosx, wb).astype(bf)
    imag = (-mixed("kn,nyz->kyz", sinx, wb)).astype(bf)
    for form, cosv, sinv in (("ky,xyz->xkz", cosy, siny), ("kz,xyz->xyk", cosz, sinz)):
        new_real = (mixed(form, cosv, real) + mixed(form, sinv, imag)).astype(bf)
        imag = (mixed(form, cosv, imag) - mixed(form, sinv, real)).astype(bf)
        real = new_real
    real = (real.astype(jnp.float32) * green_spectrum).astype(bf)
    imag = (imag.astype(jnp.float32) * green_spectrum).astype(bf)
    icosz, isinz = angle_tables(bz, bz, 0, bz, 1.0 / bz)
    icosy, isiny = angle_tables(by, by, 0, by, 1.0 / by)
    icosx, isinx = angle_tables(bx, bx, 0, bx, 1.0 / bx)
    for form, cosv, sinv in (("nk,xyk->xyn", icosz, isinz), ("nk,xkz->xnz", icosy, isiny)):
        new_real = (mixed(form, cosv, real) - mixed(form, sinv, imag)).astype(bf)
        imag = (mixed(form, cosv, imag) + mixed(form, sinv, real)).astype(bf)
        real = new_real
    return mixed("nk,kyz->nyz", icosx, real) - mixed("nk,kyz->nyz", isinx, imag)


def move_x(part, step):
    return from_behind(part, "gx", step)


def move_y(part, step):
    return from_behind(part, "gy", step)


def move_z(part, step):
    return from_behind(part, "gz", step)


def fold_margin(field, dim, mover):
    quarter = field.shape[dim] // 4
    low_rim = lax.slice_in_dim(field, 0, quarter, axis=dim)
    first = lax.slice_in_dim(field, quarter, 2 * quarter, axis=dim)
    second = lax.slice_in_dim(field, 2 * quarter, 3 * quarter, axis=dim)
    high_rim = lax.slice_in_dim(field, 3 * quarter, 4 * quarter, axis=dim)
    low_rim, high_rim = lax.optimization_barrier((low_rim, high_rim))
    from_left = mover(high_rim, 1)
    from_right = mover(low_rim, -1)
    return jnp.concatenate([first + from_left, second + from_right], axis=dim)


def gather_rows(value, axes):
    count = lax.axis_size(axes)
    width = max(value.shape[0], (1 << 18) // count)
    padded = jnp.concatenate([value, jnp.zeros((width - value.shape[0],), value.dtype)])
    return lax.all_gather(padded, axes)[:, : value.shape[0]]


def level_sums(rows, me, first_level, group_of):
    slots = lax.iota(jnp.int32, rows.shape[0])
    total = jnp.zeros(rows.shape[1:], rows.dtype)
    for level in range(1, rows.shape[0].bit_length()):
        mask = (slots >> level) == (me >> level)
        total = total + jnp.sum(jnp.where(mask[:, None], rows, 0.0), axis=0) / math.sqrt(group_of(level))
    return total


def far_sum(flat):
    nz = lax.axis_size("gz")
    zlevels = nz.bit_length() - 1
    line = gather_rows(flat, "gz")
    total = level_sums(line, lax.axis_index("gz"), 1, lambda level: 2**level)
    line_sum = jnp.sum(line, axis=0)
    plane = gather_rows(line_sum, ("gx", "gy"))
    ab = lax.axis_index(("gx", "gy"))
    return total + level_sums(plane, ab, 1, lambda level: 2 ** (level + zlevels))


def local(vorticity, green_spectrum, coupling):
    px, py, pz = (PX, PY, PZ)
    patch = vorticity.reshape(px, py, pz)
    spectrum = green_spectrum.reshape(2 * px, 2 * py, 2 * pz)
    box = local_box(patch, spectrum)
    order = ((2, move_z), (1, move_y), (0, move_x))
    near = box
    for dim, mover in order:
        near = fold_margin(near, dim, mover)
    cx, cy, cz = (px // CB, py // CB, pz // CB)
    scale = 1.0 / math.sqrt(CB**3)
    coarse = patch.reshape(cx, CB, cy, CB, cz, CB).sum(axis=(1, 3, 5)) * scale
    flat = coarse.reshape(-1)
    total = far_sum(flat)
    far = total.reshape(cx, cy, cz) * coupling
    far_cells = jnp.broadcast_to(far[:, None, :, None, :, None], (cx, CB, cy, CB, cz, CB)).reshape(
        px, py, pz
    )
    return (near + far_cells).reshape(1, 1, 1, px * py * pz)


def solution(mesh):
    return jax.shard_map(
        local,
        mesh=mesh,
        in_specs=(P("gx", "gy", "gz", None), P(), P()),
        out_specs=P("gx", "gy", "gz", None),
        check_vma=False,
    )
```

```python
import math

import jax
import jax.numpy as jnp
from jax import lax
from jax.sharding import PartitionSpec as P

PX = 32
PY = 32
PZ = 32
CB = 16


def from_behind(block, axis, distance):
    devices = range(lax.axis_size(axis))
    route = [(i - distance, i) for i in devices if i - distance in devices]
    return lax.ppermute(block, axis, route)


def from_partner(value, axis, apart):
    mask = 2**apart
    pairs = [(source, source ^ mask) for source in range(lax.axis_size(axis))]
    return lax.ppermute(value, axis, pairs)


def angle_tables(count_out, count_in, offset, length, factor):
    rows = lax.iota(jnp.int32, count_out)[:, None]
    cols = lax.iota(jnp.int32, count_in)[None, :]
    phase = (rows * (cols + offset) % length).astype(jnp.float32) * (2.0 * math.pi / length)
    return (
        (jnp.cos(phase) * factor).astype(jnp.bfloat16),
        (jnp.sin(phase) * factor).astype(jnp.bfloat16),
    )


def mixed(form, table, data):
    return jnp.einsum(form, table, data, preferred_element_type=jnp.float32)


def local_box(patch, green_spectrum):
    bf = jnp.bfloat16
    px, py, pz = patch.shape
    bx, by, bz = green_spectrum.shape
    wb = patch.astype(bf)
    cosx, sinx = angle_tables(bx, px, px // 2, bx, 1.0)
    cosy, siny = angle_tables(by, py, py // 2, by, 1.0)
    cosz, sinz = angle_tables(bz, pz, pz // 2, bz, 1.0)
    real = mixed("kn,nyz->kyz", cosx, wb).astype(bf)
    imag = (-mixed("kn,nyz->kyz", sinx, wb)).astype(bf)
    for form, cosv, sinv in (("ky,xyz->xkz", cosy, siny), ("kz,xyz->xyk", cosz, sinz)):
        new_real = (mixed(form, cosv, real) + mixed(form, sinv, imag)).astype(bf)
        imag = (mixed(form, cosv, imag) - mixed(form, sinv, real)).astype(bf)
        real = new_real
    real = (real.astype(jnp.float32) * green_spectrum).astype(bf)
    imag = (imag.astype(jnp.float32) * green_spectrum).astype(bf)
    icosz, isinz = angle_tables(bz, bz, 0, bz, 1.0 / bz)
    icosy, isiny = angle_tables(by, by, 0, by, 1.0 / by)
    icosx, isinx = angle_tables(bx, bx, 0, bx, 1.0 / bx)
    for form, cosv, sinv in (("nk,xyk->xyn", icosz, isinz), ("nk,xkz->xnz", icosy, isiny)):
        new_real = (mixed(form, cosv, real) - mixed(form, sinv, imag)).astype(bf)
        imag = (mixed(form, cosv, imag) + mixed(form, sinv, real)).astype(bf)
        real = new_real
    return mixed("nk,kyz->nyz", icosx, real) - mixed("nk,kyz->nyz", isinx, imag)


def move_x(part, step):
    return from_behind(part, "gx", step)


def move_y(part, step):
    return from_behind(part, "gy", step)


def move_z(part, step):
    return from_behind(part, "gz", step)


def fold_margin(field, dim, mover):
    quarter = field.shape[dim] // 4
    low_rim = lax.slice_in_dim(field, 0, quarter, axis=dim)
    first = lax.slice_in_dim(field, quarter, 2 * quarter, axis=dim)
    second = lax.slice_in_dim(field, 2 * quarter, 3 * quarter, axis=dim)
    high_rim = lax.slice_in_dim(field, 3 * quarter, 4 * quarter, axis=dim)
    shape = low_rim.shape
    low_rim, high_rim = (rim.reshape(-1, 128) for rim in (low_rim, high_rim))
    low_rim, high_rim = lax.optimization_barrier((low_rim, high_rim))
    from_left = mover(high_rim, 1).reshape(shape)
    from_right = mover(low_rim, -1).reshape(shape)
    return jnp.concatenate([first + from_left, second + from_right], axis=dim)


def gather_rows(value, axes):
    count = lax.axis_size(axes)
    rows = jnp.broadcast_to(value[None, :], (count, value.shape[0]))
    return lax.all_to_all(rows, axes, 0, 0, tiled=True)


def level_sums(rows, me, first_level, group_of):
    slots = lax.iota(jnp.int32, rows.shape[0])
    total = jnp.zeros(rows.shape[1:], rows.dtype)
    for level in range(1, rows.shape[0].bit_length()):
        mask = (slots >> level) == (me >> level)
        total = total + jnp.sum(jnp.where(mask[:, None], rows, 0.0), axis=0) / math.sqrt(group_of(level))
    return total


def far_sum(flat):
    nz = lax.axis_size("gz")
    zlevels = nz.bit_length() - 1
    line = gather_rows(flat, "gz")
    total = level_sums(line, lax.axis_index("gz"), 1, lambda level: 2**level)
    line_sum = jnp.sum(line, axis=0)
    plane = gather_rows(line_sum, ("gx", "gy"))
    ab = lax.axis_index(("gx", "gy"))
    return total + level_sums(plane, ab, 1, lambda level: 2 ** (level + zlevels))


def local(vorticity, green_spectrum, coupling):
    px, py, pz = (PX, PY, PZ)
    patch = vorticity.reshape(px, py, pz)
    spectrum = green_spectrum.reshape(2 * px, 2 * py, 2 * pz)
    box = local_box(patch, spectrum)
    order = ((2, move_z), (1, move_y), (0, move_x))
    near = box
    for dim, mover in order:
        near = fold_margin(near, dim, mover)
    cx, cy, cz = (px // CB, py // CB, pz // CB)
    scale = 1.0 / math.sqrt(CB**3)
    coarse = patch.reshape(cx, CB, cy, CB, cz, CB).sum(axis=(1, 3, 5)) * scale
    flat = coarse.reshape(-1)
    total = far_sum(flat)
    far = total.reshape(cx, cy, cz) * coupling
    far_cells = jnp.broadcast_to(far[:, None, :, None, :, None], (cx, CB, cy, CB, cz, CB)).reshape(
        px, py, pz
    )
    return (near + far_cells).reshape(1, 1, 1, px * py * pz)


def solution(mesh):
    return jax.shard_map(
        local,
        mesh=mesh,
        in_specs=(P("gx", "gy", "gz", None), P(), P()),
        out_specs=P("gx", "gy", "gz", None),
        check_vma=False,
    )
```

```python
import math

import jax
import jax.numpy as jnp
from jax import lax
from jax.sharding import PartitionSpec as P

PX = 32
PY = 32
PZ = 32
CB = 16


def from_behind(block, axis, distance):
    devices = range(lax.axis_size(axis))
    route = [(i - distance, i) for i in devices if i - distance in devices]
    return lax.ppermute(block, axis, route)


def from_partner(value, axis, apart):
    mask = 2**apart
    pairs = [(source, source ^ mask) for source in range(lax.axis_size(axis))]
    return lax.ppermute(value, axis, pairs)


def angle_tables(count_out, count_in, offset, length, factor):
    rows = lax.iota(jnp.int32, count_out)[:, None]
    cols = lax.iota(jnp.int32, count_in)[None, :]
    phase = (rows * (cols + offset) % length).astype(jnp.float32) * (2.0 * math.pi / length)
    return (
        (jnp.cos(phase) * factor).astype(jnp.bfloat16),
        (jnp.sin(phase) * factor).astype(jnp.bfloat16),
    )


def mixed(form, table, data):
    return jnp.einsum(form, table, data, preferred_element_type=jnp.float32)


def local_box(patch, green_spectrum):
    bf = jnp.bfloat16
    px, py, pz = patch.shape
    bx, by, bz = green_spectrum.shape
    wb = patch.astype(bf)
    cosx, sinx = angle_tables(bx, px, px // 2, bx, 1.0)
    cosy, siny = angle_tables(by, py, py // 2, by, 1.0)
    cosz, sinz = angle_tables(bz, pz, pz // 2, bz, 1.0)
    real = mixed("kn,nyz->kyz", cosx, wb).astype(bf)
    imag = (-mixed("kn,nyz->kyz", sinx, wb)).astype(bf)
    for form, cosv, sinv in (("ky,xyz->xkz", cosy, siny), ("kz,xyz->xyk", cosz, sinz)):
        new_real = (mixed(form, cosv, real) + mixed(form, sinv, imag)).astype(bf)
        imag = (mixed(form, cosv, imag) - mixed(form, sinv, real)).astype(bf)
        real = new_real
    real = (real.astype(jnp.float32) * green_spectrum).astype(bf)
    imag = (imag.astype(jnp.float32) * green_spectrum).astype(bf)
    icosz, isinz = angle_tables(bz, bz, 0, bz, 1.0 / bz)
    icosy, isiny = angle_tables(by, by, 0, by, 1.0 / by)
    icosx, isinx = angle_tables(bx, bx, 0, bx, 1.0 / bx)
    for form, cosv, sinv in (("nk,xyk->xyn", icosz, isinz), ("nk,xkz->xnz", icosy, isiny)):
        new_real = (mixed(form, cosv, real) - mixed(form, sinv, imag)).astype(bf)
        imag = (mixed(form, cosv, imag) + mixed(form, sinv, real)).astype(bf)
        real = new_real
    return mixed("nk,kyz->nyz", icosx, real) - mixed("nk,kyz->nyz", isinx, imag)


def move_x(part, step):
    return from_behind(part, "gx", step)


def move_y(part, step):
    return from_behind(part, "gy", step)


def move_z(part, step):
    return from_behind(part, "gz", step)


def fold_margin(field, dim, mover, dense):
    quarter = field.shape[dim] // 4
    low_rim = lax.slice_in_dim(field, 0, quarter, axis=dim)
    first = lax.slice_in_dim(field, quarter, 2 * quarter, axis=dim)
    second = lax.slice_in_dim(field, 2 * quarter, 3 * quarter, axis=dim)
    high_rim = lax.slice_in_dim(field, 3 * quarter, 4 * quarter, axis=dim)
    shape = low_rim.shape
    if dense:
        low_rim, high_rim = (rim.reshape(-1, 128) for rim in (low_rim, high_rim))
    low_rim, high_rim = lax.optimization_barrier((low_rim, high_rim))
    from_left = mover(high_rim, 1).reshape(shape)
    from_right = mover(low_rim, -1).reshape(shape)
    return jnp.concatenate([first + from_left, second + from_right], axis=dim)


def gather_rows(value, axes):
    count = lax.axis_size(axes)
    rows = jnp.broadcast_to(value[None, :], (count, value.shape[0]))
    return lax.all_to_all(rows, axes, 0, 0, tiled=True)


def level_sums(rows, me, first_level, group_of):
    slots = lax.iota(jnp.int32, rows.shape[0])
    total = jnp.zeros(rows.shape[1:], rows.dtype)
    for level in range(1, rows.shape[0].bit_length()):
        mask = (slots >> level) == (me >> level)
        total = total + jnp.sum(jnp.where(mask[:, None], rows, 0.0), axis=0) / math.sqrt(group_of(level))
    return total


def far_sum(flat):
    nz = lax.axis_size("gz")
    zlevels = nz.bit_length() - 1
    line = gather_rows(flat, "gz")
    total = level_sums(line, lax.axis_index("gz"), 1, lambda level: 2**level)
    line_sum = jnp.sum(line, axis=0)
    plane = gather_rows(line_sum, ("gx", "gy"))
    ab = lax.axis_index(("gx", "gy"))
    return total + level_sums(plane, ab, 1, lambda level: 2 ** (level + zlevels))


def local(vorticity, green_spectrum, coupling):
    px, py, pz = (PX, PY, PZ)
    patch = vorticity.reshape(px, py, pz)
    spectrum = green_spectrum.reshape(2 * px, 2 * py, 2 * pz)
    box = local_box(patch, spectrum)
    order = ((2, move_z), (1, move_y), (0, move_x))
    near = box
    for dim, mover in order:
        near = fold_margin(near, dim, mover, dim != 2)
    cx, cy, cz = (px // CB, py // CB, pz // CB)
    scale = 1.0 / math.sqrt(CB**3)
    coarse = patch.reshape(cx, CB, cy, CB, cz, CB).sum(axis=(1, 3, 5)) * scale
    flat = coarse.reshape(-1)
    total = far_sum(flat)
    far = total.reshape(cx, cy, cz) * coupling
    far_cells = jnp.broadcast_to(far[:, None, :, None, :, None], (cx, CB, cy, CB, cz, CB)).reshape(
        px, py, pz
    )
    return (near + far_cells).reshape(1, 1, 1, px * py * pz)


def solution(mesh):
    return jax.shard_map(
        local,
        mesh=mesh,
        in_specs=(P("gx", "gy", "gz", None), P(), P()),
        out_specs=P("gx", "gy", "gz", None),
        check_vma=False,
    )
```

```python
import math

import jax
import jax.numpy as jnp
from jax import lax
from jax.sharding import PartitionSpec as P

PX = 32
PY = 32
PZ = 32
CB = 16


def from_behind(block, axis, distance):
    devices = range(lax.axis_size(axis))
    route = [(i - distance, i) for i in devices if i - distance in devices]
    return lax.ppermute(block, axis, route)


def from_partner(value, axis, apart):
    mask = 2**apart
    pairs = [(source, source ^ mask) for source in range(lax.axis_size(axis))]
    return lax.ppermute(value, axis, pairs)


def angle_tables(count_out, count_in, offset, length, factor):
    rows = lax.iota(jnp.int32, count_out)[:, None]
    cols = lax.iota(jnp.int32, count_in)[None, :]
    phase = (rows * (cols + offset) % length).astype(jnp.float32) * (2.0 * math.pi / length)
    return (
        (jnp.cos(phase) * factor).astype(jnp.bfloat16),
        (jnp.sin(phase) * factor).astype(jnp.bfloat16),
    )


def mixed(form, table, data):
    return jnp.einsum(form, table, data, preferred_element_type=jnp.float32)


def local_box(patch, green_spectrum):
    bf = jnp.bfloat16
    px, py, pz = patch.shape
    bx, by, bz = green_spectrum.shape
    wb = patch.astype(bf)
    cosx, sinx = angle_tables(bx, px, px // 2, bx, 1.0)
    cosy, siny = angle_tables(by, py, py // 2, by, 1.0)
    cosz, sinz = angle_tables(bz, pz, pz // 2, bz, 1.0)
    real = mixed("kn,nyz->kyz", cosx, wb).astype(bf)
    imag = (-mixed("kn,nyz->kyz", sinx, wb)).astype(bf)
    for form, cosv, sinv in (("ky,xyz->xkz", cosy, siny), ("kz,xyz->xyk", cosz, sinz)):
        new_real = (mixed(form, cosv, real) + mixed(form, sinv, imag)).astype(bf)
        imag = (mixed(form, cosv, imag) - mixed(form, sinv, real)).astype(bf)
        real = new_real
    real = (real.astype(jnp.float32) * green_spectrum).astype(bf)
    imag = (imag.astype(jnp.float32) * green_spectrum).astype(bf)
    icosz, isinz = angle_tables(bz, bz, 0, bz, 1.0 / bz)
    icosy, isiny = angle_tables(by, by, 0, by, 1.0 / by)
    icosx, isinx = angle_tables(bx, bx, 0, bx, 1.0 / bx)
    for form, cosv, sinv in (("nk,xyk->xyn", icosz, isinz), ("nk,xkz->xnz", icosy, isiny)):
        new_real = (mixed(form, cosv, real) - mixed(form, sinv, imag)).astype(bf)
        imag = (mixed(form, cosv, imag) + mixed(form, sinv, real)).astype(bf)
        real = new_real
    return mixed("nk,kyz->nyz", icosx, real) - mixed("nk,kyz->nyz", isinx, imag)


def move_x(part, step):
    return from_behind(part, "gx", step)


def move_y(part, step):
    return from_behind(part, "gy", step)


def move_z(part, step):
    return from_behind(part, "gz", step)


def fold_margin(field, dim, mover, dense):
    quarter = field.shape[dim] // 4
    low_rim = lax.slice_in_dim(field, 0, quarter, axis=dim)
    first = lax.slice_in_dim(field, quarter, 2 * quarter, axis=dim)
    second = lax.slice_in_dim(field, 2 * quarter, 3 * quarter, axis=dim)
    high_rim = lax.slice_in_dim(field, 3 * quarter, 4 * quarter, axis=dim)
    shape = low_rim.shape
    if dense:
        low_rim, high_rim = (rim.reshape(-1, 128) for rim in (low_rim, high_rim))
    low_rim, high_rim = lax.optimization_barrier((low_rim, high_rim))
    from_left = mover(high_rim, 1).reshape(shape)
    from_right = mover(low_rim, -1).reshape(shape)
    return jnp.concatenate([first + from_left, second + from_right], axis=dim)


def gather_rows(value, axes):
    count = lax.axis_size(axes)
    rows = jnp.broadcast_to(value[None, :], (count, value.shape[0]))
    return lax.all_to_all(rows, axes, 0, 0, tiled=True)


def level_sums(rows, me, first_level, group_of):
    slots = lax.iota(jnp.int32, rows.shape[0])
    total = jnp.zeros(rows.shape[1:], rows.dtype)
    for level in range(1, rows.shape[0].bit_length()):
        mask = (slots >> level) == (me >> level)
        total = total + jnp.sum(jnp.where(mask[:, None], rows, 0.0), axis=0) / math.sqrt(group_of(level))
    return total


def far_sum(flat):
    inner = ("gy", "gz")
    inner_levels = lax.axis_size(inner).bit_length() - 1
    line = gather_rows(flat, inner)
    total = level_sums(line, lax.axis_index(inner), 1, lambda level: 2**level)
    line_sum = jnp.sum(line, axis=0)
    plane = gather_rows(line_sum, "gx")
    return total + level_sums(plane, lax.axis_index("gx"), 1, lambda level: 2 ** (level + inner_levels))


def local(vorticity, green_spectrum, coupling):
    px, py, pz = (PX, PY, PZ)
    patch = vorticity.reshape(px, py, pz)
    spectrum = green_spectrum.reshape(2 * px, 2 * py, 2 * pz)
    box = local_box(patch, spectrum)
    order = ((2, move_z), (1, move_y), (0, move_x))
    near = box
    for dim, mover in order:
        near = fold_margin(near, dim, mover, dim != 2)
    cx, cy, cz = (px // CB, py // CB, pz // CB)
    scale = 1.0 / math.sqrt(CB**3)
    coarse = patch.reshape(cx, CB, cy, CB, cz, CB).sum(axis=(1, 3, 5)) * scale
    flat = coarse.reshape(-1)
    total = far_sum(flat)
    far = total.reshape(cx, cy, cz) * coupling
    far_cells = jnp.broadcast_to(far[:, None, :, None, :, None], (cx, CB, cy, CB, cz, CB)).reshape(
        px, py, pz
    )
    return (near + far_cells).reshape(1, 1, 1, px * py * pz)


def solution(mesh):
    return jax.shard_map(
        local,
        mesh=mesh,
        in_specs=(P("gx", "gy", "gz", None), P(), P()),
        out_specs=P("gx", "gy", "gz", None),
        check_vma=False,
    )
```

```python
import math

import jax
import jax.numpy as jnp
from jax import lax
from jax.sharding import PartitionSpec as P

PX = 32
PY = 32
PZ = 32
CB = 16


def from_behind(block, axis, distance):
    devices = range(lax.axis_size(axis))
    route = [(i - distance, i) for i in devices if i - distance in devices]
    return lax.ppermute(block, axis, route)


def from_partner(value, axis, apart):
    mask = 2**apart
    pairs = [(source, source ^ mask) for source in range(lax.axis_size(axis))]
    return lax.ppermute(value, axis, pairs)


def angle_tables(count_out, count_in, offset, length, factor):
    rows = lax.iota(jnp.int32, count_out)[:, None]
    cols = lax.iota(jnp.int32, count_in)[None, :]
    phase = (rows * (cols + offset) % length).astype(jnp.float32) * (2.0 * math.pi / length)
    return (
        (jnp.cos(phase) * factor).astype(jnp.bfloat16),
        (jnp.sin(phase) * factor).astype(jnp.bfloat16),
    )


def mixed(form, table, data):
    return jnp.einsum(form, table, data, preferred_element_type=jnp.float32)


def local_box(patch, green_spectrum):
    bf = jnp.bfloat16
    px, py, pz = patch.shape
    bx, by, bz = green_spectrum.shape
    wb = patch.astype(bf)
    cosx, sinx = angle_tables(bx, px, px // 2, bx, 1.0)
    cosy, siny = angle_tables(by, py, py // 2, by, 1.0)
    cosz, sinz = angle_tables(bz, pz, pz // 2, bz, 1.0)
    real = mixed("kn,nyz->kyz", cosx, wb).astype(bf)
    imag = (-mixed("kn,nyz->kyz", sinx, wb)).astype(bf)
    for form, cosv, sinv in (("ky,xyz->xkz", cosy, siny), ("kz,xyz->xyk", cosz, sinz)):
        new_real = (mixed(form, cosv, real) + mixed(form, sinv, imag)).astype(bf)
        imag = (mixed(form, cosv, imag) - mixed(form, sinv, real)).astype(bf)
        real = new_real
    real = (real.astype(jnp.float32) * green_spectrum).astype(bf)
    imag = (imag.astype(jnp.float32) * green_spectrum).astype(bf)
    icosz, isinz = angle_tables(bz, bz, 0, bz, 1.0 / bz)
    icosy, isiny = angle_tables(by, by, 0, by, 1.0 / by)
    icosx, isinx = angle_tables(bx, bx, 0, bx, 1.0 / bx)
    for form, cosv, sinv in (("nk,xyk->xyn", icosz, isinz), ("nk,xkz->xnz", icosy, isiny)):
        new_real = (mixed(form, cosv, real) - mixed(form, sinv, imag)).astype(bf)
        imag = (mixed(form, cosv, imag) + mixed(form, sinv, real)).astype(bf)
        real = new_real
    return mixed("nk,kyz->nyz", icosx, real) - mixed("nk,kyz->nyz", isinx, imag)


def move_x(part, step):
    return from_behind(part, "gx", step)


def move_y(part, step):
    return from_behind(part, "gy", step)


def move_z(part, step):
    return from_behind(part, "gz", step)


def fold_margin(field, dim, mover, dense):
    quarter = field.shape[dim] // 4
    low_rim = lax.slice_in_dim(field, 0, quarter, axis=dim)
    first = lax.slice_in_dim(field, quarter, 2 * quarter, axis=dim)
    second = lax.slice_in_dim(field, 2 * quarter, 3 * quarter, axis=dim)
    high_rim = lax.slice_in_dim(field, 3 * quarter, 4 * quarter, axis=dim)
    shape = low_rim.shape
    if dense:
        low_rim, high_rim = (rim.reshape(-1, 128) for rim in (low_rim, high_rim))
    low_rim, high_rim = lax.optimization_barrier((low_rim, high_rim))
    from_left = mover(high_rim, 1).reshape(shape)
    from_right = mover(low_rim, -1).reshape(shape)
    return jnp.concatenate([first + from_left, second + from_right], axis=dim)


def gather_rows(value, axes, groups=None):
    count = lax.axis_size(axes) if groups is None else len(groups[0])
    rows = jnp.broadcast_to(value[None, :], (count, value.shape[0]))
    return lax.all_to_all(rows, axes, 0, 0, tiled=True, axis_index_groups=groups)


def level_sums(rows, me, first_level, group_of):
    slots = lax.iota(jnp.int32, rows.shape[0])
    total = jnp.zeros(rows.shape[1:], rows.dtype)
    for level in range(1, rows.shape[0].bit_length()):
        mask = (slots >> level) == (me >> level)
        total = total + jnp.sum(jnp.where(mask[:, None], rows, 0.0), axis=0) / math.sqrt(group_of(level))
    return total


def line_sums(flat):
    nz = lax.axis_size("gz")
    c = lax.axis_index("gz")
    near = 4
    groups = [[start + i for i in range(near)] for start in range(0, nz, near)]
    local_rows = gather_rows(flat, "gz", groups)
    total = level_sums(local_rows, c % near, 1, lambda level: 2**level)
    strided = [[start + near * i for i in range(nz // near)] for start in range(near)]
    group_rows = gather_rows(jnp.sum(local_rows, axis=0), "gz", strided)
    total = total + level_sums(group_rows, c // near, 1, lambda level: near * 2**level)
    return total, jnp.sum(group_rows, axis=0)


def plane_sums(total, line_sum):
    zlevels = lax.axis_size("gz").bit_length() - 1
    plane = gather_rows(line_sum, ("gx", "gy"))
    ab = lax.axis_index(("gx", "gy"))
    return total + level_sums(plane, ab, 1, lambda level: 2 ** (level + zlevels))


def local(vorticity, green_spectrum, coupling):
    px, py, pz = (PX, PY, PZ)
    patch = vorticity.reshape(px, py, pz)
    spectrum = green_spectrum.reshape(2 * px, 2 * py, 2 * pz)
    cx, cy, cz = (px // CB, py // CB, pz // CB)
    scale = 1.0 / math.sqrt(CB**3)
    coarse = patch.reshape(cx, CB, cy, CB, cz, CB).sum(axis=(1, 3, 5)) * scale
    flat = coarse.reshape(-1)
    partial, line_sum = line_sums(flat)
    partial, line_sum, patch = lax.optimization_barrier((partial, line_sum, patch))
    box = local_box(patch, spectrum)
    order = ((2, move_z), (1, move_y), (0, move_x))
    near = box
    for dim, mover in order:
        near = fold_margin(near, dim, mover, dim != 2)
    total = plane_sums(partial, line_sum)
    far = total.reshape(cx, cy, cz) * coupling
    far_cells = jnp.broadcast_to(far[:, None, :, None, :, None], (cx, CB, cy, CB, cz, CB)).reshape(
        px, py, pz
    )
    return (near + far_cells).reshape(1, 1, 1, px * py * pz)


def solution(mesh):
    return jax.shard_map(
        local,
        mesh=mesh,
        in_specs=(P("gx", "gy", "gz", None), P(), P()),
        out_specs=P("gx", "gy", "gz", None),
        check_vma=False,
    )
```

```python
import math

import jax
import jax.numpy as jnp
from jax import lax
from jax.sharding import PartitionSpec as P

PX = 32
PY = 32
PZ = 32
CB = 16


def from_behind(block, axis, distance):
    devices = range(lax.axis_size(axis))
    route = [(i - distance, i) for i in devices if i - distance in devices]
    return lax.ppermute(block, axis, route)


def from_partner(value, axis, apart):
    mask = 2**apart
    pairs = [(source, source ^ mask) for source in range(lax.axis_size(axis))]
    return lax.ppermute(value, axis, pairs)


def angle_tables(count_out, count_in, offset, length, factor):
    rows = lax.iota(jnp.int32, count_out)[:, None]
    cols = lax.iota(jnp.int32, count_in)[None, :]
    phase = (rows * (cols + offset) % length).astype(jnp.float32) * (2.0 * math.pi / length)
    return (
        (jnp.cos(phase) * factor).astype(jnp.bfloat16),
        (jnp.sin(phase) * factor).astype(jnp.bfloat16),
    )


def mixed(form, table, data):
    return jnp.einsum(form, table, data, preferred_element_type=jnp.float32)


def local_box(patch, green_spectrum):
    bf = jnp.bfloat16
    px, py, pz = patch.shape
    bx, by, bz = green_spectrum.shape
    wb = patch.astype(bf)
    cosx, sinx = angle_tables(bx, px, px // 2, bx, 1.0)
    cosy, siny = angle_tables(by, py, py // 2, by, 1.0)
    cosz, sinz = angle_tables(bz, pz, pz // 2, bz, 1.0)
    real = mixed("kn,nyz->kyz", cosx, wb).astype(bf)
    imag = (-mixed("kn,nyz->kyz", sinx, wb)).astype(bf)
    for form, cosv, sinv in (("ky,xyz->xkz", cosy, siny), ("kz,xyz->xyk", cosz, sinz)):
        new_real = (mixed(form, cosv, real) + mixed(form, sinv, imag)).astype(bf)
        imag = (mixed(form, cosv, imag) - mixed(form, sinv, real)).astype(bf)
        real = new_real
    real = (real.astype(jnp.float32) * green_spectrum).astype(bf)
    imag = (imag.astype(jnp.float32) * green_spectrum).astype(bf)
    icosz, isinz = angle_tables(bz, bz, 0, bz, 1.0 / bz)
    icosy, isiny = angle_tables(by, by, 0, by, 1.0 / by)
    icosx, isinx = angle_tables(bx, bx, 0, bx, 1.0 / bx)
    for form, cosv, sinv in (("nk,xyk->xyn", icosz, isinz), ("nk,xkz->xnz", icosy, isiny)):
        new_real = (mixed(form, cosv, real) - mixed(form, sinv, imag)).astype(bf)
        imag = (mixed(form, cosv, imag) + mixed(form, sinv, real)).astype(bf)
        real = new_real
    return mixed("nk,kyz->nyz", icosx, real) - mixed("nk,kyz->nyz", isinx, imag)


def move_x(part, step):
    return from_behind(part, "gx", step)


def move_y(part, step):
    return from_behind(part, "gy", step)


def move_z(part, step):
    return from_behind(part, "gz", step)


def fold_margin(field, dim, mover, dense):
    quarter = field.shape[dim] // 4
    low_rim = lax.slice_in_dim(field, 0, quarter, axis=dim)
    first = lax.slice_in_dim(field, quarter, 2 * quarter, axis=dim)
    second = lax.slice_in_dim(field, 2 * quarter, 3 * quarter, axis=dim)
    high_rim = lax.slice_in_dim(field, 3 * quarter, 4 * quarter, axis=dim)
    shape = low_rim.shape
    if dense:
        low_rim, high_rim = (rim.reshape(-1, 128) for rim in (low_rim, high_rim))
    low_rim, high_rim = lax.optimization_barrier((low_rim, high_rim))
    from_left = mover(high_rim, 1).reshape(shape)
    from_right = mover(low_rim, -1).reshape(shape)
    return jnp.concatenate([first + from_left, second + from_right], axis=dim)


def gather_rows(value, axes):
    count = lax.axis_size(axes)
    rows = jnp.broadcast_to(value[None, :], (count, value.shape[0]))
    return lax.all_to_all(rows, axes, 0, 0, tiled=True)


def level_sums(rows, me, first_level, group_of):
    slots = lax.iota(jnp.int32, rows.shape[0])
    total = jnp.zeros(rows.shape[1:], rows.dtype)
    for level in range(1, rows.shape[0].bit_length()):
        mask = (slots >> level) == (me >> level)
        total = total + jnp.sum(jnp.where(mask[:, None], rows, 0.0), axis=0) / math.sqrt(group_of(level))
    return total


def far_sum(flat):
    nz = lax.axis_size("gz")
    zlevels = nz.bit_length() - 1
    line = gather_rows(flat, "gz")
    total = level_sums(line, lax.axis_index("gz"), 1, lambda level: 2**level)
    line_sum = jnp.sum(line, axis=0)
    plane = gather_rows(line_sum, ("gx", "gy"))
    ab = lax.axis_index(("gx", "gy"))
    return total + level_sums(plane, ab, 1, lambda level: 2 ** (level + zlevels))


def local(vorticity, green_spectrum, coupling):
    px, py, pz = (PX, PY, PZ)
    patch = vorticity.reshape(px, py, pz)
    spectrum = green_spectrum.reshape(2 * px, 2 * py, 2 * pz)
    box = local_box(patch, spectrum)
    order = ((2, move_z), (1, move_y), (0, move_x))
    near = box
    for dim, mover in order:
        near = fold_margin(near, dim, mover, dim != 2)
    cx, cy, cz = (px // CB, py // CB, pz // CB)
    scale = 1.0 / math.sqrt(CB**3)
    lanes = 128 // pz
    rows = vorticity.reshape(cx, CB, cy, py // cy // lanes, lanes * pz).sum(axis=(1, 3))
    coarse = rows.reshape(cx, cy, lanes, cz, CB).sum(axis=(2, 4)) * scale
    flat = coarse.reshape(-1)
    total = far_sum(flat)
    far = total.reshape(cx, cy, cz) * coupling
    far_cells = jnp.broadcast_to(far[:, None, :, None, :, None], (cx, CB, cy, CB, cz, CB)).reshape(
        px, py, pz
    )
    return (near + far_cells).reshape(1, 1, 1, px * py * pz)


def solution(mesh):
    return jax.shard_map(
        local,
        mesh=mesh,
        in_specs=(P("gx", "gy", "gz", None), P(), P()),
        out_specs=P("gx", "gy", "gz", None),
        check_vma=False,
    )
```
